512 devices in a mesh: shard: 128 (over y, z, core), tensor: 4 (over x).
Axes of the slice: x: 4, y: 8, z: 8, core: 2. Of those that a mesh axis runs over, the one named last changes fastest.
Arguments:
- big_grad: bfloat16 [32, 1280, 768], P(None, 'shard', 'tensor')
- big_weight: bfloat16 [32, 1280, 768], P(None, 'shard', 'tensor'), may hold values from -0.017944336 to 0.017944336
- big_moment: float32 [128, 768, 1280], P('shard', 'tensor'), may hold values from -6 to 6
- small_grad: bfloat16 [32, 1280, 192], P(None, 'shard')
- small_weight: bfloat16 [32, 1280, 192], P(None, 'shard'), may hold values from -0.15625 to 0.15625
- small_moment: float32 [128, 192, 1280], P('shard'), may hold values from -6 to 6
- owners: int32 [2, 32], replicated, may hold values from 0 to 127, as said below
- vec_parts: float32 [128, 43008], P('shard'), may hold values from -0.6 to 0.6
- vec_param: float32 [43008], P('shard'), may hold values from 0.5 to 1.5
- vec_first: float32 [43008], P('shard'), may hold values from -0.6 to 0.6
- vec_second: float32 [43008], P('shard'), may hold values from 0.01 to 1
Outputs:
- big_weight_new: bfloat16 [32, 1280, 768], P(None, 'shard', 'tensor')
- big_moment_new: float32 [128, 768, 1280], P('shard', 'tensor')
- small_weight_new: bfloat16 [32, 1280, 192], P(None, 'shard')
- small_moment_new: float32 [128, 192, 1280], P('shard')
- vec_param_new: float32 [43008], P('shard')
- vec_first_new: float32 [43008], P('shard')
- vec_second_new: float32 [43008], P('shard')
The draws below stay inside these ranges and needn't reach their ends.
Inputs may be any that keep to these rules, and one draw needn't show every extreme that they name: `owners`: no shard index appears twice in the whole list (over both rows); each aligned group of four shard indices holds exactly one owner of each row; the first and the last shard index own a matrix.
All inputs are finite; a program needn't handle non-finite values.
Results may differ from the reference program's by a relative error of at most 0.0068.
Values may be sent and summed in bfloat16 or wider, within the bound.
No kernel may reach another device: no remote copies, remote signals or barrier semaphores. Data moves between devices by JAX's collectives and lax.ppermute only.
A program may use at most 64 MiB of HBM per device.

```python
import math
import jax
import jax.numpy as jnp
from jax import lax

D = 1280
ITERS = 2
QW = 768
KVW = 192
BIG = 32
VEC = 43008
N_SHARD = 128


def scaled_field(key, shape):
    first_key = jax.random.fold_in(key, 1)
    second_key = jax.random.fold_in(key, 2)
    third_key = jax.random.fold_in(key, 3)
    base = jnp.clip(jax.random.normal(first_key, shape, jnp.float32), -4.0, 4.0)
    row_scale = 10.0 ** jax.random.uniform(second_key, (shape[0], shape[1], 1), jnp.float32, -0.5, 0.5)
    column_scale = 10.0 ** jax.random.uniform(third_key, (shape[0], 1, shape[2]), jnp.float32, -0.5, 0.5)
    return base * row_scale * column_scale


def layered_field(key, shape):
    matrices = shape[0]
    strong_terms = 16
    medium_terms = 48
    terms = strong_terms + medium_terms
    left_int = jax.random.randint(jax.random.fold_in(key, 41), (matrices, shape[1], terms), -128, 129).astype(jnp.int32)
    strong_amp = jax.random.randint(jax.random.fold_in(key, 42), (matrices, strong_terms, 1), 96, 129).astype(jnp.int32)
    medium_amp = jax.random.randint(jax.random.fold_in(key, 43), (matrices, medium_terms, 1), 40, 57).astype(jnp.int32)
    amplitude = jnp.concatenate([strong_amp, medium_amp], axis=1)
    right_unit = jax.random.randint(jax.random.fold_in(key, 44), (matrices, terms, shape[2]), -128, 129).astype(jnp.int32)
    right_int = right_unit * amplitude // 128
    product = lax.dot_general(left_int.astype(jnp.float32), right_int.astype(jnp.float32), (((2,), (1,)), ((0,), (0,))), precision=lax.Precision.HIGHEST)
    low = product * 0.0001220703125
    column_scale = 10.0 ** jax.random.uniform(jax.random.fold_in(key, 46), (matrices, 1, shape[2]), jnp.float32, -0.5, 0.5)
    row_scale = 10.0 ** jax.random.uniform(jax.random.fold_in(key, 47), (matrices, shape[1], 1), jnp.float32, -0.5, 0.5)
    overall = 0.5
    return overall * low * row_scale * column_scale


def draw_big_grad(key, part):
    return layered_field(jax.random.fold_in(key, 11), (BIG, D, QW)).astype(jnp.bfloat16)


def draw_small_grad(key, part):
    return scaled_field(jax.random.fold_in(key, 13), (BIG, D, KVW)).astype(jnp.bfloat16)


def draw_owners(key, part):
    groups = BIG
    group_index = jnp.arange(groups, dtype=jnp.int32)
    first_offset = jax.random.randint(jax.random.fold_in(key, 31), (groups,), 0, 4).astype(jnp.int32)
    first_offset = jnp.where(group_index == 0, 0, jnp.where(group_index == groups - 1, 3, first_offset))
    step_offset = jax.random.randint(jax.random.fold_in(key, 32), (groups,), 1, 4).astype(jnp.int32)
    second_offset = (first_offset + step_offset) % 4
    first_order = jax.random.permutation(jax.random.fold_in(key, 33), groups).astype(jnp.int32)
    second_order = jax.random.permutation(jax.random.fold_in(key, 34), groups).astype(jnp.int32)
    first_row = first_order * 4 + jnp.take(first_offset, first_order)
    second_row = second_order * 4 + jnp.take(second_offset, second_order)
    return jnp.stack([first_row, second_row]).astype(jnp.int32)


def steps_of(own_key, extent, pieces, least, high):
    level, own = 1.0, jax.random.fold_in(own_key, 6)
    for dim, blocks in pieces:
        heights = jnp.exp(jax.random.uniform(jax.random.fold_in(own, dim), (blocks,), jnp.float32, least / len(pieces), high / len(pieces)))
        level = level * jnp.repeat(heights, extent[dim] // blocks).reshape([-1 if axis == dim else 1 for axis in range(len(extent))])
    return level


def normal_values(own_key, dims, deviation, most, shards=(), kind=jnp.bfloat16):
    entries = jax.random.normal(own_key, dims, jnp.float32) * deviation
    if len(shards) > 0:
        entries = steps_of(own_key, dims, shards, -0.22, 0.18) * entries
    return jnp.clip(entries, min=-most, max=most).astype(kind)


def setup_inputs(seed: int = 0) -> dict:
    arg_keys = jax.random.split(jax.random.key(seed), 12)
    return {
        "big_grad": draw_big_grad(jax.random.fold_in(arg_keys[11], 71), 0),
        "big_weight": normal_values(arg_keys[1], (BIG, D, QW), 0.003, 0.017944336, ((1, 128), (2, 4))),
        "big_moment": normal_values(arg_keys[2], (N_SHARD, QW, D), 1.0, 6.0, ((0, 128), (1, 4)), jnp.float32),
        "small_grad": draw_small_grad(jax.random.fold_in(arg_keys[11], 71), 0),
        "small_weight": normal_values(arg_keys[4], (BIG, D, KVW), D ** -0.5, 0.15625, ((1, 128),)),
        "small_moment": normal_values(arg_keys[5], (N_SHARD, KVW, D), 1.0, 6.0, ((0, 128),), jnp.float32),
        "owners": draw_owners(jax.random.fold_in(arg_keys[11], 71), 0),
        "vec_parts": normal_values(arg_keys[7], (N_SHARD, VEC), 0.1, 0.6, ((0, 128),), jnp.float32),
        "vec_param": jnp.clip(1.0 + 0.1 * jax.random.normal(arg_keys[8], (VEC,), jnp.float32), 0.5, 1.5),
        "vec_first": normal_values(arg_keys[9], (VEC,), 0.1, 0.6, ((0, 128),), jnp.float32),
        "vec_second": jnp.clip(jnp.exp(math.log(1.0) - 4.6051702 * jax.random.uniform(arg_keys[10], (VEC,), jnp.float32) ** steps_of(arg_keys[10], (VEC,), ((0, 128),), -0.2, 0.2)), 0.01, 1.0),
    }


newton_linear = 3.4445
newton_cubic = -4.775
newton_quintic = 2.0315
momentum_rate = 0.95
muon_rate = 0.05
weight_decay = 0.1
norm_epsilon = 1e-07
adam_rate = 0.004
first_decay = 0.9
second_decay = 0.95
adam_epsilon = 1e-08
first_correct = 0.99997343860111
second_correct = 0.99407947077967

def normalized(field):
    values = field.astype(jnp.float32)
    squares = jnp.sum(values * values)
    return (values / (jnp.sqrt(squares) + norm_epsilon)).astype(jnp.bfloat16)

def gram_block(left_part, right_part):
    product = lax.dot_general(left_part.astype(jnp.float32), right_part.astype(jnp.float32), (((0,), (0,)), ((), ())))
    return product.astype(jnp.bfloat16)

def poly_block(gram_part, gram_full):
    square = jnp.dot(gram_part, gram_full, preferred_element_type=jnp.float32)
    return (newton_cubic * gram_part.astype(jnp.float32) + newton_quintic * square).astype(jnp.bfloat16)

def newton_step(column_part, full_iterate, polynomial):
    product = lax.dot_general(full_iterate.astype(jnp.float32), polynomial.astype(jnp.float32), (((1,), (1,)), ((), ())))
    return (newton_linear * column_part.astype(jnp.float32) + product).astype(jnp.bfloat16)

def orthogonal(field):
    iterate = normalized(field)
    for iteration in range(ITERS):
        gram_full = gram_block(iterate, iterate)
        iterate = newton_step(iterate, iterate, poly_block(gram_full, gram_full))
    return iterate

def apply_update(weight, update):
    scale = 0.2 * math.sqrt(D)
    values = weight.astype(jnp.float32)
    return (values - muon_rate * (scale * update.astype(jnp.float32) + weight_decay * values)).astype(jnp.bfloat16)

def update_kind(gradients, weights, moments, owner_indices):

    def update_one(packed):
        gradient, weight, owner_index = packed
        previous = lax.dynamic_index_in_dim(moments, owner_index.astype(jnp.int32), 0, keepdims=False).T
        values = gradient.astype(jnp.float32)
        renewed = momentum_rate * previous + values
        blended = (values + momentum_rate * renewed).astype(jnp.bfloat16)
        return (apply_update(weight, orthogonal(blended)), renewed)
    new_weights, renewed_all = lax.map(update_one, (gradients, weights, owner_indices))
    new_moments = moments.at[owner_indices.astype(jnp.int32)].set(jnp.swapaxes(renewed_all, 1, 2))
    return (new_weights, new_moments)

def reference(big_grad, big_weight, big_moment, small_grad, small_weight, small_moment, owners, vec_parts, vec_param, vec_first, vec_second):
    big_weight_new, big_moment_new = update_kind(big_grad, big_weight, big_moment, owners[0])
    small_weight_new, small_moment_new = update_kind(small_grad, small_weight, small_moment, owners[1])
    gain_grad = lax.optimization_barrier(jnp.sum(vec_parts, axis=0))
    first_new = first_decay * vec_first + (1.0 - first_decay) * gain_grad
    second_new = second_decay * vec_second + (1.0 - second_decay) * gain_grad * gain_grad
    param_new = vec_param - adam_rate * (first_new / first_correct) / (jnp.sqrt(second_new / second_correct) + adam_epsilon)
    return (big_weight_new, big_moment_new, small_weight_new, small_moment_new, param_new, first_new, second_new)
```

```python
import math

import jax
import jax.numpy as jnp
from jax import lax
from jax.sharding import PartitionSpec as P

D = 1280
ITERS = 2


newton_linear = 3.4445
newton_cubic = -4.775
newton_quintic = 2.0315
momentum_rate = 0.95
muon_rate = 0.05
weight_decay = 0.1
norm_epsilon = 1e-07
adam_rate = 0.004
first_decay = 0.9
second_decay = 0.95
adam_epsilon = 1e-08
first_correct = 0.99997343860111
second_correct = 0.99407947077967


def owner_table(owner_list, count):
    devices = lax.broadcasted_iota(jnp.int32, (count, owner_list.shape[0]), 0)
    return (devices == owner_list[None, :]).astype(jnp.bfloat16)


def route_rows(owner_map, pieces):
    flattened = pieces.reshape(pieces.shape[0], -1)
    routed = jnp.dot(owner_map, flattened, preferred_element_type=jnp.float32)
    return routed.astype(jnp.bfloat16).reshape((owner_map.shape[0],) + pieces.shape[1:])


def collect(owner_map, arrived):
    flattened = arrived.reshape(arrived.shape[0], -1)
    picked = lax.dot_general(
        owner_map, flattened, (((0,), (0,)), ((), ())), preferred_element_type=jnp.float32
    )
    return picked.astype(jnp.bfloat16).reshape((owner_map.shape[1],) + arrived.shape[1:])


def advance(arrived, moment, is_owner):
    gradient = arrived.T.astype(jnp.float32)
    renewed = momentum_rate * moment + gradient
    retained = jnp.where(is_owner, renewed, moment)
    blended = jnp.where(is_owner, gradient + momentum_rate * renewed, 0.0).astype(jnp.bfloat16).T
    return (retained, blended)


def normalized(field):
    values = field.astype(jnp.float32)
    squares = jnp.sum(values * values)
    return (values / (jnp.sqrt(squares) + norm_epsilon)).astype(jnp.bfloat16)


def gram_block(left_part, right_part):
    product = lax.dot_general(
        left_part, right_part, (((0,), (0,)), ((), ())), preferred_element_type=jnp.float32
    )
    return product.astype(jnp.bfloat16)


def poly_block(gram_part, gram_full):
    square = jnp.dot(gram_part, gram_full, preferred_element_type=jnp.float32)
    return (newton_cubic * gram_part.astype(jnp.float32) + newton_quintic * square).astype(
        jnp.bfloat16
    )


def newton_step(column_part, full_iterate, polynomial):
    product = lax.dot_general(
        full_iterate, polynomial, (((1,), (1,)), ((), ())), preferred_element_type=jnp.float32
    )
    return (newton_linear * column_part.astype(jnp.float32) + product).astype(jnp.bfloat16)


def small_newton(field):
    iterate = normalized(field)
    for iteration in range(ITERS):
        gram_full = gram_block(iterate, iterate)
        iterate = newton_step(iterate, iterate, poly_block(gram_full, gram_full))
    return iterate


def apply_update(weight, update):
    scale = 0.2 * math.sqrt(D)
    values = weight.astype(jnp.float32)
    return (
        values - muon_rate * (scale * update.astype(jnp.float32) + weight_decay * values)
    ).astype(jnp.bfloat16)


def gather_columns(column_part):
    return lax.all_gather(column_part, "tensor", axis=1, tiled=True)


def gather_gram(gram_part):
    return lax.all_gather(gram_part, "tensor", axis=0, tiled=True)


def per_device(
    big_grad,
    big_weight,
    big_moment,
    small_grad,
    small_weight,
    small_moment,
    owners,
    vec_parts,
    vec_param,
    vec_first,
    vec_second,
):
    shards = lax.axis_size("shard")
    shard_place = lax.axis_index("shard")
    column = lax.axis_index("tensor")
    block_width = big_grad.shape[2]
    rows_dev = big_grad.shape[1]
    matrices = big_grad.shape[0]
    joint_map = owner_table(jnp.concatenate([owners[0], owners[1]]), shards)
    joint_pieces = jnp.concatenate([big_grad, small_grad], axis=0)
    arrived = lax.all_to_all(
        route_rows(joint_map, joint_pieces), "shard", split_axis=0, concat_axis=1, tiled=True
    )[0]
    big_owner = jnp.any(owners[0] == shard_place)
    small_owner = jnp.any(owners[1] == shard_place)
    big_retained, big_blended = advance(arrived, big_moment[0], big_owner)
    small_retained, small_blended = advance(arrived, small_moment[0], small_owner)
    small_result = small_newton(small_blended)
    full_iterate = normalized(gather_columns(big_blended))
    for iteration in range(ITERS - 1):
        gram_full = gram_block(full_iterate, full_iterate)
        full_iterate = newton_step(full_iterate, full_iterate, poly_block(gram_full, gram_full))
    gram_full = gram_block(full_iterate, full_iterate)
    gram_rows = lax.dynamic_slice_in_dim(gram_full, column * block_width, block_width, 0)
    owned_part = lax.dynamic_slice_in_dim(full_iterate, column * block_width, block_width, 1)
    big_result = newton_step(owned_part, full_iterate, poly_block(gram_rows, gram_full))
    own_result = jnp.where(big_owner, big_result, small_result)
    returned = lax.all_to_all(
        own_result.reshape(shards, rows_dev, block_width),
        "shard",
        split_axis=0,
        concat_axis=0,
        tiled=True,
    )
    picked = collect(joint_map, returned)
    big_weight_new = apply_update(big_weight, picked[:matrices])
    small_weight_new = apply_update(small_weight, picked[matrices:])
    vec_pieces = vec_parts[0].reshape(shards, -1)
    grad_share = jnp.sum(
        lax.all_to_all(vec_pieces, "shard", split_axis=0, concat_axis=0, tiled=True), axis=0
    )
    first_new = first_decay * vec_first + (1.0 - first_decay) * grad_share
    second_new = second_decay * vec_second + (1.0 - second_decay) * grad_share * grad_share
    param_new = vec_param - adam_rate * (first_new / first_correct) / (
        jnp.sqrt(second_new / second_correct) + adam_epsilon
    )
    return (
        big_weight_new,
        big_retained[None],
        small_weight_new,
        small_retained[None],
        param_new,
        first_new,
        second_new,
    )


def solution(mesh):
    return jax.shard_map(
        per_device,
        mesh=mesh,
        in_specs=(
            P(None, "shard", "tensor"),
            P(None, "shard", "tensor"),
            P("shard", "tensor", None),
            P(None, "shard", None),
            P(None, "shard", None),
            P("shard", None, None),
            P(),
            P("shard", None),
            P("shard"),
            P("shard"),
            P("shard"),
        ),
        out_specs=(
            P(None, "shard", "tensor"),
            P("shard", "tensor", None),
            P(None, "shard", None),
            P("shard", None, None),
            P("shard"),
            P("shard"),
            P("shard"),
        ),
        check_vma=False,
    )
```

```python
import math

import jax
import jax.numpy as jnp
from jax import lax
from jax.sharding import PartitionSpec as P

D = 1280
ITERS = 2


newton_linear = 3.4445
newton_cubic = -4.775
newton_quintic = 2.0315
momentum_rate = 0.95
muon_rate = 0.05
weight_decay = 0.1
norm_epsilon = 1e-07
adam_rate = 0.004
first_decay = 0.9
second_decay = 0.95
adam_epsilon = 1e-08
first_correct = 0.99997343860111
second_correct = 0.99407947077967


def owner_table(owner_list, count):
    devices = lax.broadcasted_iota(jnp.int32, (count, owner_list.shape[0]), 0)
    return (devices == owner_list[None, :]).astype(jnp.bfloat16)


def route_rows(owner_map, pieces):
    flattened = pieces.reshape(pieces.shape[0], -1)
    routed = jnp.dot(owner_map, flattened, preferred_element_type=jnp.float32)
    return routed.astype(jnp.bfloat16).reshape((owner_map.shape[0],) + pieces.shape[1:])


def collect(owner_map, arrived):
    flattened = arrived.reshape(arrived.shape[0], -1)
    picked = lax.dot_general(
        owner_map, flattened, (((0,), (0,)), ((), ())), preferred_element_type=jnp.float32
    )
    return picked.astype(jnp.bfloat16).reshape((owner_map.shape[1],) + arrived.shape[1:])


def advance(arrived, moment, is_owner):
    gradient = arrived.T.astype(jnp.float32)
    renewed = momentum_rate * moment + gradient
    retained = jnp.where(is_owner, renewed, moment)
    blended = jnp.where(is_owner, gradient + momentum_rate * renewed, 0.0).astype(jnp.bfloat16).T
    return (retained, blended)


def normalized(field):
    values = field.astype(jnp.float32)
    squares = jnp.sum(values * values)
    return (values / (jnp.sqrt(squares) + norm_epsilon)).astype(jnp.bfloat16)


def gram_block(left_part, right_part):
    product = lax.dot_general(
        left_part, right_part, (((0,), (0,)), ((), ())), preferred_element_type=jnp.float32
    )
    return product.astype(jnp.bfloat16)


def poly_block(gram_part, gram_full):
    square = jnp.dot(gram_part, gram_full, preferred_element_type=jnp.float32)
    return (newton_cubic * gram_part.astype(jnp.float32) + newton_quintic * square).astype(
        jnp.bfloat16
    )


def newton_step(column_part, full_iterate, polynomial):
    product = lax.dot_general(
        full_iterate, polynomial, (((1,), (1,)), ((), ())), preferred_element_type=jnp.float32
    )
    return (newton_linear * column_part.astype(jnp.float32) + product).astype(jnp.bfloat16)


def small_newton(field):
    iterate = normalized(field)
    for iteration in range(ITERS):
        gram_full = gram_block(iterate, iterate)
        iterate = newton_step(iterate, iterate, poly_block(gram_full, gram_full))
    return iterate


def apply_update(weight, update):
    scale = 0.2 * math.sqrt(D)
    values = weight.astype(jnp.float32)
    return (
        values - muon_rate * (scale * update.astype(jnp.float32) + weight_decay * values)
    ).astype(jnp.bfloat16)


def gather_columns(column_part):
    count = lax.axis_size("tensor")
    blocks = [column_part]
    for shift in range(1, count):
        blocks.append(
            lax.ppermute(column_part, "tensor", [(i, (i + shift) % count) for i in range(count)])
        )
    return jnp.concatenate(blocks, axis=1)


def gather_gram(gram_part):
    return lax.all_gather(gram_part, "tensor", axis=0, tiled=True)


def per_device(
    big_grad,
    big_weight,
    big_moment,
    small_grad,
    small_weight,
    small_moment,
    owners,
    vec_parts,
    vec_param,
    vec_first,
    vec_second,
):
    shards = lax.axis_size("shard")
    shard_place = lax.axis_index("shard")
    column = lax.axis_index("tensor")
    block_width = big_grad.shape[2]
    rows_dev = big_grad.shape[1]
    matrices = big_grad.shape[0]
    joint_map = owner_table(jnp.concatenate([owners[0], owners[1]]), shards)
    joint_pieces = jnp.concatenate([big_grad, small_grad], axis=0)
    arrived = lax.all_to_all(
        route_rows(joint_map, joint_pieces), "shard", split_axis=0, concat_axis=1, tiled=True
    )[0]
    big_owner = jnp.any(owners[0] == shard_place)
    small_owner = jnp.any(owners[1] == shard_place)
    big_retained, big_blended = advance(arrived, big_moment[0], big_owner)
    small_retained, small_blended = advance(arrived, small_moment[0], small_owner)
    small_result = small_newton(small_blended)
    full_iterate = normalized(gather_columns(big_blended))
    for iteration in range(ITERS - 1):
        gram_full = gram_block(full_iterate, full_iterate)
        full_iterate = newton_step(full_iterate, full_iterate, poly_block(gram_full, gram_full))
    gram_full = gram_block(full_iterate, full_iterate)
    gram_rows = gram_full[:block_width]
    owned_part = full_iterate[:, :block_width]
    big_result = newton_step(owned_part, full_iterate, poly_block(gram_rows, gram_full))
    own_result = jnp.where(big_owner, big_result, small_result)
    returned = lax.all_to_all(
        own_result.reshape(shards, rows_dev, block_width),
        "shard",
        split_axis=0,
        concat_axis=0,
        tiled=True,
    )
    picked = collect(joint_map, returned)
    big_weight_new = apply_update(big_weight, picked[:matrices])
    small_weight_new = apply_update(small_weight, picked[matrices:])
    vec_pieces = vec_parts[0].reshape(shards, -1)
    grad_share = jnp.sum(
        lax.all_to_all(vec_pieces, "shard", split_axis=0, concat_axis=0, tiled=True), axis=0
    )
    first_new = first_decay * vec_first + (1.0 - first_decay) * grad_share
    second_new = second_decay * vec_second + (1.0 - second_decay) * grad_share * grad_share
    param_new = vec_param - adam_rate * (first_new / first_correct) / (
        jnp.sqrt(second_new / second_correct) + adam_epsilon
    )
    return (
        big_weight_new,
        big_retained[None],
        small_weight_new,
        small_retained[None],
        param_new,
        first_new,
        second_new,
    )


def solution(mesh):
    return jax.shard_map(
        per_device,
        mesh=mesh,
        in_specs=(
            P(None, "shard", "tensor"),
            P(None, "shard", "tensor"),
            P("shard", "tensor", None),
            P(None, "shard", None),
            P(None, "shard", None),
            P("shard", None, None),
            P(),
            P("shard", None),
            P("shard"),
            P("shard"),
            P("shard"),
        ),
        out_specs=(
            P(None, "shard", "tensor"),
            P("shard", "tensor", None),
            P(None, "shard", None),
            P("shard", None, None),
            P("shard"),
            P("shard"),
            P("shard"),
        ),
        check_vma=False,
    )
```

```python
import math

import jax
import jax.numpy as jnp
from jax import lax
from jax.sharding import PartitionSpec as P

D = 1280
ITERS = 2


newton_linear = 3.4445
newton_cubic = -4.775
newton_quintic = 2.0315
momentum_rate = 0.95
muon_rate = 0.05
weight_decay = 0.1
norm_epsilon = 1e-07
adam_rate = 0.004
first_decay = 0.9
second_decay = 0.95
adam_epsilon = 1e-08
first_correct = 0.99997343860111
second_correct = 0.99407947077967


def owner_table(owner_list, count):
    devices = lax.broadcasted_iota(jnp.int32, (count, owner_list.shape[0]), 0)
    return (devices == owner_list[None, :]).astype(jnp.bfloat16)


def route_rows(owner_map, pieces):
    flattened = pieces.reshape(pieces.shape[0], -1)
    routed = jnp.dot(owner_map, flattened, preferred_element_type=jnp.float32)
    return routed.astype(jnp.bfloat16).reshape((owner_map.shape[0],) + pieces.shape[1:])


def collect(owner_map, arrived):
    flattened = arrived.reshape(arrived.shape[0], -1)
    picked = lax.dot_general(
        owner_map, flattened, (((0,), (0,)), ((), ())), preferred_element_type=jnp.float32
    )
    return picked.astype(jnp.bfloat16).reshape((owner_map.shape[1],) + arrived.shape[1:])


def advance(arrived, moment, is_owner):
    gradient = arrived.T.astype(jnp.float32)
    renewed = momentum_rate * moment + gradient
    retained = jnp.where(is_owner, renewed, moment)
    blended = jnp.where(is_owner, gradient + momentum_rate * renewed, 0.0).astype(jnp.bfloat16).T
    return (retained, blended)


def normalized(field):
    values = field.astype(jnp.float32)
    squares = jnp.sum(values * values)
    return (values / (jnp.sqrt(squares) + norm_epsilon)).astype(jnp.bfloat16)


def gram_block(left_part, right_part):
    product = lax.dot_general(
        left_part, right_part, (((0,), (0,)), ((), ())), preferred_element_type=jnp.float32
    )
    return product.astype(jnp.bfloat16)


def poly_block(gram_part, gram_full):
    square = jnp.dot(gram_part, gram_full, preferred_element_type=jnp.float32)
    return (newton_cubic * gram_part.astype(jnp.float32) + newton_quintic * square).astype(
        jnp.bfloat16
    )


def newton_step(column_part, full_iterate, polynomial):
    product = lax.dot_general(
        full_iterate, polynomial, (((1,), (1,)), ((), ())), preferred_element_type=jnp.float32
    )
    return (newton_linear * column_part.astype(jnp.float32) + product).astype(jnp.bfloat16)


def small_newton(field):
    iterate = normalized(field)
    for iteration in range(ITERS):
        gram_full = gram_block(iterate, iterate)
        iterate = newton_step(iterate, iterate, poly_block(gram_full, gram_full))
    return iterate


def apply_update(weight, update):
    scale = 0.2 * math.sqrt(D)
    values = weight.astype(jnp.float32)
    return (
        values - muon_rate * (scale * update.astype(jnp.float32) + weight_decay * values)
    ).astype(jnp.bfloat16)


def gather_columns(column_part):
    count = lax.axis_size("tensor")
    ahead = [(i, (i + 1) % count) for i in range(count)]
    behind = [(i, (i - 1) % count) for i in range(count)]
    from_behind = lax.ppermute(column_part, "tensor", ahead)
    from_ahead = lax.ppermute(column_part, "tensor", behind)
    half = column_part.shape[0] // 2
    far = jnp.concatenate(
        [
            lax.ppermute(from_behind[:half], "tensor", ahead),
            lax.ppermute(from_ahead[half:], "tensor", behind),
        ],
        axis=0,
    )
    return jnp.concatenate([column_part, from_behind, far, from_ahead], axis=1)


def gather_gram(gram_part):
    return lax.all_gather(gram_part, "tensor", axis=0, tiled=True)


def per_device(
    big_grad,
    big_weight,
    big_moment,
    small_grad,
    small_weight,
    small_moment,
    owners,
    vec_parts,
    vec_param,
    vec_first,
    vec_second,
):
    shards = lax.axis_size("shard")
    shard_place = lax.axis_index("shard")
    column = lax.axis_index("tensor")
    block_width = big_grad.shape[2]
    rows_dev = big_grad.shape[1]
    matrices = big_grad.shape[0]
    joint_map = owner_table(jnp.concatenate([owners[0], owners[1]]), shards)
    joint_pieces = jnp.concatenate([big_grad, small_grad], axis=0)
    routed = route_rows(joint_map, joint_pieces).reshape(shards, -1)
    vec_values = vec_parts[0]
    vec_high = lax.reduce_precision(vec_values, exponent_bits=8, mantissa_bits=7)
    vec_low = vec_values - vec_high
    outgoing = jnp.concatenate(
        [
            routed,
            vec_high.astype(jnp.bfloat16).reshape(shards, -1),
            vec_low.astype(jnp.bfloat16).reshape(shards, -1),
        ],
        axis=1,
    )
    incoming = lax.all_to_all(outgoing, "shard", split_axis=0, concat_axis=0, tiled=True)
    routed_width = routed.shape[1]
    vec_width = vec_values.shape[0] // shards
    arrived = incoming[:, :routed_width].reshape(shards * rows_dev, block_width)
    vec_in = incoming[:, routed_width:].astype(jnp.float32)
    grad_share = jnp.sum(vec_in[:, :vec_width] + vec_in[:, vec_width:], axis=0)
    big_owner = jnp.any(owners[0] == shard_place)
    small_owner = jnp.any(owners[1] == shard_place)
    big_retained, big_blended = advance(arrived, big_moment[0], big_owner)
    small_retained, small_blended = advance(arrived, small_moment[0], small_owner)
    small_result = small_newton(small_blended)
    full_iterate = normalized(gather_columns(big_blended))
    for iteration in range(ITERS - 1):
        gram_full = gram_block(full_iterate, full_iterate)
        full_iterate = newton_step(full_iterate, full_iterate, poly_block(gram_full, gram_full))
    gram_full = gram_block(full_iterate, full_iterate)
    gram_rows = gram_full[:block_width]
    owned_part = full_iterate[:, :block_width]
    big_result = newton_step(owned_part, full_iterate, poly_block(gram_rows, gram_full))
    own_result = jnp.where(big_owner, big_result, small_result)
    returned = lax.all_to_all(
        own_result.reshape(shards, rows_dev, block_width),
        "shard",
        split_axis=0,
        concat_axis=0,
        tiled=True,
    )
    picked = collect(joint_map, returned)
    big_weight_new = apply_update(big_weight, picked[:matrices])
    small_weight_new = apply_update(small_weight, picked[matrices:])
    first_new = first_decay * vec_first + (1.0 - first_decay) * grad_share
    second_new = second_decay * vec_second + (1.0 - second_decay) * grad_share * grad_share
    param_new = vec_param - adam_rate * (first_new / first_correct) / (
        jnp.sqrt(second_new / second_correct) + adam_epsilon
    )
    return (
        big_weight_new,
        big_retained[None],
        small_weight_new,
        small_retained[None],
        param_new,
        first_new,
        second_new,
    )


def solution(mesh):
    return jax.shard_map(
        per_device,
        mesh=mesh,
        in_specs=(
            P(None, "shard", "tensor"),
            P(None, "shard", "tensor"),
            P("shard", "tensor", None),
            P(None, "shard", None),
            P(None, "shard", None),
            P("shard", None, None),
            P(),
            P("shard", None),
            P("shard"),
            P("shard"),
            P("shard"),
        ),
        out_specs=(
            P(None, "shard", "tensor"),
            P("shard", "tensor", None),
            P(None, "shard", None),
            P("shard", None, None),
            P("shard"),
            P("shard"),
            P("shard"),
        ),
        check_vma=False,
    )
```

```python
import math

import jax
import jax.numpy as jnp
from jax import lax
from jax.sharding import PartitionSpec as P

D = 1280
ITERS = 2


newton_linear = 3.4445
newton_cubic = -4.775
newton_quintic = 2.0315
momentum_rate = 0.95
muon_rate = 0.05
weight_decay = 0.1
norm_epsilon = 1e-07
adam_rate = 0.004
first_decay = 0.9
second_decay = 0.95
adam_epsilon = 1e-08
first_correct = 0.99997343860111
second_correct = 0.99407947077967


def owner_table(owner_list, count):
    devices = lax.broadcasted_iota(jnp.int32, (count, owner_list.shape[0]), 0)
    return (devices == owner_list[None, :]).astype(jnp.bfloat16)


def route_rows(owner_map, pieces):
    flattened = pieces.reshape(pieces.shape[0], -1)
    routed = jnp.dot(owner_map, flattened, preferred_element_type=jnp.float32)
    return routed.astype(jnp.bfloat16).reshape((owner_map.shape[0],) + pieces.shape[1:])


def collect(owner_map, arrived):
    flattened = arrived.reshape(arrived.shape[0], -1)
    picked = lax.dot_general(
        owner_map, flattened, (((0,), (0,)), ((), ())), preferred_element_type=jnp.float32
    )
    return picked.astype(jnp.bfloat16).reshape((owner_map.shape[1],) + arrived.shape[1:])


def advance(arrived, moment, is_owner):
    gradient = arrived.T.astype(jnp.float32)
    renewed = momentum_rate * moment + gradient
    retained = jnp.where(is_owner, renewed, moment)
    blended = jnp.where(is_owner, gradient + momentum_rate * renewed, 0.0).astype(jnp.bfloat16).T
    return (retained, blended)


def normalized(field):
    values = field.astype(jnp.float32)
    squares = jnp.sum(values * values)
    return (values / (jnp.sqrt(squares) + norm_epsilon)).astype(jnp.bfloat16)


def gram_block(left_part, right_part):
    product = lax.dot_general(
        left_part, right_part, (((0,), (0,)), ((), ())), preferred_element_type=jnp.float32
    )
    return product.astype(jnp.bfloat16)


def poly_block(gram_part, gram_full):
    square = jnp.dot(gram_part, gram_full, preferred_element_type=jnp.float32)
    return (newton_cubic * gram_part.astype(jnp.float32) + newton_quintic * square).astype(
        jnp.bfloat16
    )


def newton_step(column_part, full_iterate, polynomial):
    product = lax.dot_general(
        full_iterate, polynomial, (((1,), (1,)), ((), ())), preferred_element_type=jnp.float32
    )
    return (newton_linear * column_part.astype(jnp.float32) + product).astype(jnp.bfloat16)


def small_newton(field):
    iterate = normalized(field)
    for iteration in range(ITERS):
        gram_full = gram_block(iterate, iterate)
        iterate = newton_step(iterate, iterate, poly_block(gram_full, gram_full))
    return iterate


def apply_update(weight, update):
    scale = 0.2 * math.sqrt(D)
    values = weight.astype(jnp.float32)
    return (
        values - muon_rate * (scale * update.astype(jnp.float32) + weight_decay * values)
    ).astype(jnp.bfloat16)


def gather_columns(column_part, rider):
    count = lax.axis_size("tensor")
    ahead = [(i, (i + 1) % count) for i in range(count)]
    behind = [(i, (i - 1) % count) for i in range(count)]
    from_behind = lax.ppermute(column_part, "tensor", ahead)
    from_ahead = lax.ppermute(column_part, "tensor", behind)
    from_behind, from_ahead, rider = lax.optimization_barrier((from_behind, from_ahead, rider))
    half = column_part.shape[1] // 2
    far_first = lax.ppermute(from_behind[:, :half], "tensor", ahead)
    far_second = lax.ppermute(from_ahead[:, half:], "tensor", behind)
    gathered = jnp.concatenate(
        [column_part, from_behind, far_first, far_second, from_ahead], axis=1
    )
    return gathered, rider


def gather_gram(gram_part):
    return lax.all_gather(gram_part, "tensor", axis=0, tiled=True)


def per_device(
    big_grad,
    big_weight,
    big_moment,
    small_grad,
    small_weight,
    small_moment,
    owners,
    vec_parts,
    vec_param,
    vec_first,
    vec_second,
):
    shards = lax.axis_size("shard")
    shard_place = lax.axis_index("shard")
    column = lax.axis_index("tensor")
    block_width = big_grad.shape[2]
    rows_dev = big_grad.shape[1]
    matrices = big_grad.shape[0]
    joint_map = owner_table(jnp.concatenate([owners[0], owners[1]]), shards)
    joint_pieces = jnp.concatenate([big_grad, small_grad], axis=0)
    arrived = lax.all_to_all(
        route_rows(joint_map, joint_pieces), "shard", split_axis=0, concat_axis=1, tiled=True
    )[0]
    big_owner = jnp.any(owners[0] == shard_place)
    small_owner = jnp.any(owners[1] == shard_place)
    big_retained, big_blended = advance(arrived, big_moment[0], big_owner)
    small_retained, small_blended = advance(arrived, small_moment[0], small_owner)
    small_result = small_newton(small_blended)
    gathered, vec_pieces = gather_columns(big_blended, vec_parts[0].reshape(shards, -1))
    full_iterate = normalized(gathered)
    grad_share = jnp.sum(
        lax.all_to_all(vec_pieces, "shard", split_axis=0, concat_axis=0, tiled=True), axis=0
    )
    for iteration in range(ITERS - 1):
        gram_full = gram_block(full_iterate, full_iterate)
        full_iterate = newton_step(full_iterate, full_iterate, poly_block(gram_full, gram_full))
    gram_full = gram_block(full_iterate, full_iterate)
    gram_rows = gram_full[:block_width]
    owned_part = full_iterate[:, :block_width]
    big_result = newton_step(owned_part, full_iterate, poly_block(gram_rows, gram_full))
    own_result = jnp.where(big_owner, big_result, small_result)
    returned = lax.all_to_all(
        own_result.reshape(shards, rows_dev, block_width),
        "shard",
        split_axis=0,
        concat_axis=0,
        tiled=True,
    )
    picked = collect(joint_map, returned)
    big_weight_new = apply_update(big_weight, picked[:matrices])
    small_weight_new = apply_update(small_weight, picked[matrices:])
    first_new = first_decay * vec_first + (1.0 - first_decay) * grad_share
    second_new = second_decay * vec_second + (1.0 - second_decay) * grad_share * grad_share
    param_new = vec_param - adam_rate * (first_new / first_correct) / (
        jnp.sqrt(second_new / second_correct) + adam_epsilon
    )
    return (
        big_weight_new,
        big_retained[None],
        small_weight_new,
        small_retained[None],
        param_new,
        first_new,
        second_new,
    )


def solution(mesh):
    return jax.shard_map(
        per_device,
        mesh=mesh,
        in_specs=(
            P(None, "shard", "tensor"),
            P(None, "shard", "tensor"),
            P("shard", "tensor", None),
            P(None, "shard", None),
            P(None, "shard", None),
            P("shard", None, None),
            P(),
            P("shard", None),
            P("shard"),
            P("shard"),
            P("shard"),
        ),
        out_specs=(
            P(None, "shard", "tensor"),
            P("shard", "tensor", None),
            P(None, "shard", None),
            P("shard", None, None),
            P("shard"),
            P("shard"),
            P("shard"),
        ),
        check_vma=False,
    )
```

```python
import math

import jax
import jax.numpy as jnp
from jax import lax
from jax.sharding import PartitionSpec as P

D = 1280
ITERS = 2


newton_linear = 3.4445
newton_cubic = -4.775
newton_quintic = 2.0315
momentum_rate = 0.95
muon_rate = 0.05
weight_decay = 0.1
norm_epsilon = 1e-07
adam_rate = 0.004
first_decay = 0.9
second_decay = 0.95
adam_epsilon = 1e-08
first_correct = 0.99997343860111
second_correct = 0.99407947077967


def owner_table(owner_list, count):
    devices = lax.broadcasted_iota(jnp.int32, (count, owner_list.shape[0]), 0)
    return (devices == owner_list[None, :]).astype(jnp.bfloat16)


def route_rows(owner_map, pieces):
    flattened = pieces.reshape(pieces.shape[0], -1)
    routed = jnp.dot(owner_map, flattened, preferred_element_type=jnp.float32)
    return routed.astype(jnp.bfloat16).reshape((owner_map.shape[0],) + pieces.shape[1:])


def collect(owner_map, arrived):
    flattened = arrived.reshape(arrived.shape[0], -1)
    picked = lax.dot_general(
        owner_map, flattened, (((0,), (0,)), ((), ())), preferred_element_type=jnp.float32
    )
    return picked.astype(jnp.bfloat16).reshape((owner_map.shape[1],) + arrived.shape[1:])


def advance(arrived, moment, is_owner):
    gradient = arrived.T.astype(jnp.float32)
    renewed = momentum_rate * moment + gradient
    blended = jnp.where(is_owner, gradient + momentum_rate * renewed, 0.0).astype(jnp.bfloat16).T
    return blended


def retain(arrived, moment, is_owner):
    arrived, moment = lax.optimization_barrier((arrived, moment))
    renewed = momentum_rate * moment + arrived.T.astype(jnp.float32)
    return jnp.where(is_owner, renewed, moment)


def normalized(field):
    values = field.astype(jnp.float32)
    squares = jnp.sum(values * values)
    return (values / (jnp.sqrt(squares) + norm_epsilon)).astype(jnp.bfloat16)


def gram_block(left_part, right_part):
    product = lax.dot_general(
        left_part, right_part, (((0,), (0,)), ((), ())), preferred_element_type=jnp.float32
    )
    return product.astype(jnp.bfloat16)


def poly_block(gram_part, gram_full):
    square = jnp.dot(gram_part, gram_full, preferred_element_type=jnp.float32)
    return (newton_cubic * gram_part.astype(jnp.float32) + newton_quintic * square).astype(
        jnp.bfloat16
    )


def newton_step(column_part, full_iterate, polynomial):
    product = lax.dot_general(
        full_iterate, polynomial, (((1,), (1,)), ((), ())), preferred_element_type=jnp.float32
    )
    return (newton_linear * column_part.astype(jnp.float32) + product).astype(jnp.bfloat16)


def small_newton(field):
    iterate = normalized(field)
    for iteration in range(ITERS):
        gram_full = gram_block(iterate, iterate)
        iterate = newton_step(iterate, iterate, poly_block(gram_full, gram_full))
    return iterate


def apply_update(weight, update):
    scale = 0.2 * math.sqrt(D)
    values = weight.astype(jnp.float32)
    return (
        values - muon_rate * (scale * update.astype(jnp.float32) + weight_decay * values)
    ).astype(jnp.bfloat16)


def gather_columns(column_part, rider):
    count = lax.axis_size("tensor")
    ahead = [(i, (i + 1) % count) for i in range(count)]
    behind = [(i, (i - 1) % count) for i in range(count)]
    from_behind = lax.ppermute(column_part, "tensor", ahead)
    from_ahead = lax.ppermute(column_part, "tensor", behind)
    from_behind, from_ahead, rider = lax.optimization_barrier((from_behind, from_ahead, rider))
    half = column_part.shape[1] // 2
    far_first = lax.ppermute(from_behind[:, :half], "tensor", ahead)
    far_second = lax.ppermute(from_ahead[:, half:], "tensor", behind)
    gathered = jnp.concatenate(
        [column_part, from_behind, far_first, far_second, from_ahead], axis=1
    )
    return gathered, rider


def gather_gram(gram_part):
    return lax.all_gather(gram_part, "tensor", axis=0, tiled=True)


def per_device(
    big_grad,
    big_weight,
    big_moment,
    small_grad,
    small_weight,
    small_moment,
    owners,
    vec_parts,
    vec_param,
    vec_first,
    vec_second,
):
    shards = lax.axis_size("shard")
    shard_place = lax.axis_index("shard")
    column = lax.axis_index("tensor")
    block_width = big_grad.shape[2]
    rows_dev = big_grad.shape[1]
    matrices = big_grad.shape[0]
    joint_map = owner_table(jnp.concatenate([owners[0], owners[1]]), shards)
    joint_pieces = jnp.concatenate([big_grad, small_grad], axis=0)
    arrived = lax.all_to_all(
        route_rows(joint_map, joint_pieces), "shard", split_axis=0, concat_axis=1, tiled=True
    )[0]
    big_owner = jnp.any(owners[0] == shard_place)
    small_owner = jnp.any(owners[1] == shard_place)
    big_blended = advance(arrived, big_moment[0], big_owner)
    small_blended = advance(arrived, small_moment[0], small_owner)
    big_retained = retain(arrived, big_moment[0], big_owner)
    small_retained = retain(arrived, small_moment[0], small_owner)
    small_result = small_newton(small_blended)
    gathered, vec_pieces = gather_columns(big_blended, vec_parts[0].reshape(shards, -1))
    full_iterate = normalized(gathered)
    grad_share = jnp.sum(
        lax.all_to_all(vec_pieces, "shard", split_axis=0, concat_axis=0, tiled=True), axis=0
    )
    for iteration in range(ITERS - 1):
        gram_full = gram_block(full_iterate, full_iterate)
        full_iterate = newton_step(full_iterate, full_iterate, poly_block(gram_full, gram_full))
    gram_full = gram_block(full_iterate, full_iterate)
    gram_rows = gram_full[:block_width]
    owned_part = full_iterate[:, :block_width]
    big_result = newton_step(owned_part, full_iterate, poly_block(gram_rows, gram_full))
    own_result = jnp.where(big_owner, big_result, small_result)
    returned = lax.all_to_all(
        own_result.reshape(shards, rows_dev, block_width),
        "shard",
        split_axis=0,
        concat_axis=0,
        tiled=True,
    )
    picked = collect(joint_map, returned)
    big_weight_new = apply_update(big_weight, picked[:matrices])
    small_weight_new = apply_update(small_weight, picked[matrices:])
    first_new = first_decay * vec_first + (1.0 - first_decay) * grad_share
    second_new = second_decay * vec_second + (1.0 - second_decay) * grad_share * grad_share
    param_new = vec_param - adam_rate * (first_new / first_correct) / (
        jnp.sqrt(second_new / second_correct) + adam_epsilon
    )
    return (
        big_weight_new,
        big_retained[None],
        small_weight_new,
        small_retained[None],
        param_new,
        first_new,
        second_new,
    )


def solution(mesh):
    return jax.shard_map(
        per_device,
        mesh=mesh,
        in_specs=(
            P(None, "shard", "tensor"),
            P(None, "shard", "tensor"),
            P("shard", "tensor", None),
            P(None, "shard", None),
            P(None, "shard", None),
            P("shard", None, None),
            P(),
            P("shard", None),
            P("shard"),
            P("shard"),
            P("shard"),
        ),
        out_specs=(
            P(None, "shard", "tensor"),
            P("shard", "tensor", None),
            P(None, "shard", None),
            P("shard", None, None),
            P("shard"),
            P("shard"),
            P("shard"),
        ),
        check_vma=False,
    )
```

```python
import math

import jax
import jax.numpy as jnp
from jax import lax
from jax.sharding import PartitionSpec as P

D = 1280
ITERS = 2


newton_linear = 3.4445
newton_cubic = -4.775
newton_quintic = 2.0315
momentum_rate = 0.95
muon_rate = 0.05
weight_decay = 0.1
norm_epsilon = 1e-07
adam_rate = 0.004
first_decay = 0.9
second_decay = 0.95
adam_epsilon = 1e-08
first_correct = 0.99997343860111
second_correct = 0.99407947077967


def owner_table(owner_list, count):
    devices = lax.broadcasted_iota(jnp.int32, (count, owner_list.shape[0]), 0)
    return (devices == owner_list[None, :]).astype(jnp.bfloat16)


def route_rows(owner_map, pieces):
    flattened = pieces.reshape(pieces.shape[0], -1)
    routed = jnp.dot(owner_map, flattened, preferred_element_type=jnp.float32)
    return routed.astype(jnp.bfloat16).reshape((owner_map.shape[0],) + pieces.shape[1:])


def collect(owner_map, arrived):
    flattened = arrived.reshape(arrived.shape[0], -1)
    picked = lax.dot_general(
        owner_map, flattened, (((0,), (0,)), ((), ())), preferred_element_type=jnp.float32
    )
    return picked.astype(jnp.bfloat16).reshape((owner_map.shape[1],) + arrived.shape[1:])


def advance(arrived, moment, is_owner):
    gradient = arrived.T.astype(jnp.float32)
    renewed = momentum_rate * moment + gradient
    retained = jnp.where(is_owner, renewed, moment)
    blended = jnp.where(is_owner, gradient + momentum_rate * renewed, 0.0).astype(jnp.bfloat16).T
    return (retained, blended)


def normalized(field):
    values = field.astype(jnp.float32)
    squares = jnp.sum(values * values)
    return (values / (jnp.sqrt(squares) + norm_epsilon)).astype(jnp.bfloat16)


def gram_block(left_part, right_part):
    product = lax.dot_general(
        left_part, right_part, (((0,), (0,)), ((), ())), preferred_element_type=jnp.float32
    )
    return product.astype(jnp.bfloat16)


def poly_block(gram_part, gram_full):
    square = jnp.dot(gram_part, gram_full, preferred_element_type=jnp.float32)
    return (newton_cubic * gram_part.astype(jnp.float32) + newton_quintic * square).astype(
        jnp.bfloat16
    )


def newton_step(column_part, full_iterate, polynomial):
    product = lax.dot_general(
        full_iterate, polynomial, (((1,), (1,)), ((), ())), preferred_element_type=jnp.float32
    )
    return (newton_linear * column_part.astype(jnp.float32) + product).astype(jnp.bfloat16)


def small_newton(field):
    iterate = normalized(field)
    for iteration in range(ITERS):
        gram_full = gram_block(iterate, iterate)
        iterate = newton_step(iterate, iterate, poly_block(gram_full, gram_full))
    return iterate


def apply_update(weight, update):
    scale = 0.2 * math.sqrt(D)
    values = weight.astype(jnp.float32)
    return (
        values - muon_rate * (scale * update.astype(jnp.float32) + weight_decay * values)
    ).astype(jnp.bfloat16)


def gather_columns(column_part):
    count = lax.axis_size("tensor")
    ahead = [(i, (i + 1) % count) for i in range(count)]
    behind = [(i, (i - 1) % count) for i in range(count)]
    from_behind = lax.ppermute(column_part, "tensor", ahead)
    from_ahead = lax.ppermute(column_part, "tensor", behind)
    half = column_part.shape[1] // 2
    far_first = lax.ppermute(from_behind[:, :half], "tensor", ahead)
    far_second = lax.ppermute(from_ahead[:, half:], "tensor", behind)
    gathered = jnp.concatenate(
        [column_part, from_behind, far_first, far_second, from_ahead], axis=1
    )
    return gathered


def gather_gram(gram_part):
    return lax.all_gather(gram_part, "tensor", axis=0, tiled=True)


def per_device(
    big_grad,
    big_weight,
    big_moment,
    small_grad,
    small_weight,
    small_moment,
    owners,
    vec_parts,
    vec_param,
    vec_first,
    vec_second,
):
    shards = lax.axis_size("shard")
    shard_place = lax.axis_index("shard")
    column = lax.axis_index("tensor")
    block_width = big_grad.shape[2]
    rows_dev = big_grad.shape[1]
    matrices = big_grad.shape[0]
    joint_map = owner_table(jnp.concatenate([owners[0], owners[1]]), shards)
    joint_pieces = jnp.concatenate([big_grad, small_grad], axis=0)
    routed = route_rows(joint_map, joint_pieces).reshape(shards, -1)
    outgoing = jnp.concatenate(
        [routed, vec_parts[0].astype(jnp.bfloat16).reshape(shards, -1)], axis=1
    )
    incoming = lax.all_to_all(outgoing, "shard", split_axis=0, concat_axis=0, tiled=True)
    arrived = incoming[:, : routed.shape[1]].reshape(shards * rows_dev, block_width)
    grad_share = jnp.sum(incoming[:, routed.shape[1] :].astype(jnp.float32), axis=0)
    big_owner = jnp.any(owners[0] == shard_place)
    small_owner = jnp.any(owners[1] == shard_place)
    big_retained, big_blended = advance(arrived, big_moment[0], big_owner)
    small_retained, small_blended = advance(arrived, small_moment[0], small_owner)
    small_result = small_newton(small_blended)
    full_iterate = normalized(gather_columns(big_blended))
    for iteration in range(ITERS - 1):
        gram_full = gram_block(full_iterate, full_iterate)
        full_iterate = newton_step(full_iterate, full_iterate, poly_block(gram_full, gram_full))
    gram_full = gram_block(full_iterate, full_iterate)
    gram_rows = gram_full[:block_width]
    owned_part = full_iterate[:, :block_width]
    big_result = newton_step(owned_part, full_iterate, poly_block(gram_rows, gram_full))
    own_result = jnp.where(big_owner, big_result, small_result)
    returned = lax.all_to_all(
        own_result.reshape(shards, rows_dev, block_width),
        "shard",
        split_axis=0,
        concat_axis=0,
        tiled=True,
    )
    picked = collect(joint_map, returned)
    big_weight_new = apply_update(big_weight, picked[:matrices])
    small_weight_new = apply_update(small_weight, picked[matrices:])
    first_new = first_decay * vec_first + (1.0 - first_decay) * grad_share
    second_new = second_decay * vec_second + (1.0 - second_decay) * grad_share * grad_share
    param_new = vec_param - adam_rate * (first_new / first_correct) / (
        jnp.sqrt(second_new / second_correct) + adam_epsilon
    )
    return (
        big_weight_new,
        big_retained[None],
        small_weight_new,
        small_retained[None],
        param_new,
        first_new,
        second_new,
    )


def solution(mesh):
    return jax.shard_map(
        per_device,
        mesh=mesh,
        in_specs=(
            P(None, "shard", "tensor"),
            P(None, "shard", "tensor"),
            P("shard", "tensor", None),
            P(None, "shard", None),
            P(None, "shard", None),
            P("shard", None, None),
            P(),
            P("shard", None),
            P("shard"),
            P("shard"),
            P("shard"),
        ),
        out_specs=(
            P(None, "shard", "tensor"),
            P("shard", "tensor", None),
            P(None, "shard", None),
            P("shard", None, None),
            P("shard"),
            P("shard"),
            P("shard"),
        ),
        check_vma=False,
    )
```

```python
import math

import jax
import jax.numpy as jnp
from jax import lax
from jax.sharding import PartitionSpec as P

D = 1280
ITERS = 2


newton_linear = 3.4445
newton_cubic = -4.775
newton_quintic = 2.0315
momentum_rate = 0.95
muon_rate = 0.05
weight_decay = 0.1
norm_epsilon = 1e-07
adam_rate = 0.004
first_decay = 0.9
second_decay = 0.95
adam_epsilon = 1e-08
first_correct = 0.99997343860111
second_correct = 0.99407947077967


def owner_table(owner_list, count):
    devices = lax.broadcasted_iota(jnp.int32, (count, owner_list.shape[0]), 0)
    return (devices == owner_list[None, :]).astype(jnp.bfloat16)


def route_rows(owner_map, pieces):
    flattened = pieces.reshape(pieces.shape[0], -1)
    routed = jnp.dot(owner_map, flattened, preferred_element_type=jnp.float32)
    return routed.astype(jnp.bfloat16).reshape((owner_map.shape[0],) + pieces.shape[1:])


def collect(owner_map, arrived):
    flattened = arrived.reshape(arrived.shape[0], -1)
    picked = lax.dot_general(
        owner_map, flattened, (((0,), (0,)), ((), ())), preferred_element_type=jnp.float32
    )
    return picked.astype(jnp.bfloat16).reshape((owner_map.shape[1],) + arrived.shape[1:])


def advance(arrived, moment, is_owner):
    gradient = arrived.T.astype(jnp.float32)
    renewed = momentum_rate * moment + gradient
    retained = jnp.where(is_owner, renewed, moment)
    blended = jnp.where(is_owner, gradient + momentum_rate * renewed, 0.0).astype(jnp.bfloat16).T
    return (retained, blended)


def normalized(field):
    values = field.astype(jnp.float32)
    squares = jnp.sum(values * values)
    return (values / (jnp.sqrt(squares) + norm_epsilon)).astype(jnp.bfloat16)


def gram_block(left_part, right_part):
    product = lax.dot_general(
        left_part, right_part, (((0,), (0,)), ((), ())), preferred_element_type=jnp.float32
    )
    return product.astype(jnp.bfloat16)


def poly_block(gram_part, gram_full):
    square = jnp.dot(gram_part, gram_full, preferred_element_type=jnp.float32)
    return (newton_cubic * gram_part.astype(jnp.float32) + newton_quintic * square).astype(
        jnp.bfloat16
    )


def newton_step(column_part, full_iterate, polynomial):
    product = lax.dot_general(
        full_iterate, polynomial, (((1,), (1,)), ((), ())), preferred_element_type=jnp.float32
    )
    return (newton_linear * column_part.astype(jnp.float32) + product).astype(jnp.bfloat16)


def small_newton(field):
    iterate = normalized(field)
    for iteration in range(ITERS):
        gram_full = gram_block(iterate, iterate)
        iterate = newton_step(iterate, iterate, poly_block(gram_full, gram_full))
    return iterate


def apply_update(weight, update):
    scale = 0.2 * math.sqrt(D)
    values = weight.astype(jnp.float32)
    return (
        values - muon_rate * (scale * update.astype(jnp.float32) + weight_decay * values)
    ).astype(jnp.bfloat16)


def gather_columns(column_part):
    count = lax.axis_size("tensor")
    ahead = [(i, (i + 1) % count) for i in range(count)]
    behind = [(i, (i - 1) % count) for i in range(count)]
    from_behind = lax.ppermute(column_part, "tensor", ahead)
    from_ahead = lax.ppermute(column_part, "tensor", behind)
    half = column_part.shape[1] // 2
    far_first = lax.ppermute(from_behind[:, :half], "tensor", ahead)
    far_second = lax.ppermute(from_ahead[:, half:], "tensor", behind)
    gathered = jnp.concatenate(
        [column_part, from_behind, far_first, far_second, from_ahead], axis=1
    )
    return gathered


def gather_gram(gram_part):
    return lax.all_gather(gram_part, "tensor", axis=0, tiled=True)


def per_device(
    big_grad,
    big_weight,
    big_moment,
    small_grad,
    small_weight,
    small_moment,
    owners,
    vec_parts,
    vec_param,
    vec_first,
    vec_second,
):
    shards = lax.axis_size("shard")
    shard_place = lax.axis_index("shard")
    column = lax.axis_index("tensor")
    block_width = big_grad.shape[2]
    rows_dev = big_grad.shape[1]
    matrices = big_grad.shape[0]
    owner_list = jnp.concatenate([owners[0], owners[1]])
    joint_map = owner_table(owner_list, shards)
    joint_pieces = jnp.concatenate([big_grad, small_grad], axis=0)
    listed = lax.broadcasted_iota(jnp.int32, (shards, owner_list.shape[0]), 1)
    hits = lax.broadcasted_iota(jnp.int32, (shards, owner_list.shape[0]), 0) == owner_list[None, :]
    owned_index = jnp.sum(jnp.where(hits, listed, 0), axis=1) + jnp.where(
        jnp.any(hits, axis=1), 0, owner_list.shape[0]
    )
    padded_pieces = jnp.concatenate([joint_pieces, jnp.zeros_like(joint_pieces[:1])], axis=0)
    routed = jnp.take(padded_pieces, owned_index, axis=0).reshape(shards, -1)
    outgoing = jnp.concatenate(
        [routed, vec_parts[0].astype(jnp.bfloat16).reshape(shards, -1)], axis=1
    )
    incoming = lax.all_to_all(outgoing, "shard", split_axis=0, concat_axis=0, tiled=True)
    arrived = incoming[:, : routed.shape[1]].reshape(shards * rows_dev, block_width)
    grad_share = jnp.sum(incoming[:, routed.shape[1] :].astype(jnp.float32), axis=0)
    big_owner = jnp.any(owners[0] == shard_place)
    small_owner = jnp.any(owners[1] == shard_place)
    big_retained, big_blended = advance(arrived, big_moment[0], big_owner)
    small_retained, small_blended = advance(arrived, small_moment[0], small_owner)
    small_result = small_newton(small_blended)
    full_iterate = normalized(gather_columns(big_blended))
    for iteration in range(ITERS - 1):
        gram_full = gram_block(full_iterate, full_iterate)
        full_iterate = newton_step(full_iterate, full_iterate, poly_block(gram_full, gram_full))
    gram_full = gram_block(full_iterate, full_iterate)
    gram_rows = gram_full[:block_width]
    owned_part = full_iterate[:, :block_width]
    big_result = newton_step(owned_part, full_iterate, poly_block(gram_rows, gram_full))
    own_result = jnp.where(big_owner, big_result, small_result)
    returned = lax.all_to_all(
        own_result.reshape(shards, rows_dev, block_width),
        "shard",
        split_axis=0,
        concat_axis=0,
        tiled=True,
    )
    picked = jnp.take(returned, owner_list, axis=0)
    big_weight_new = apply_update(big_weight, picked[:matrices])
    small_weight_new = apply_update(small_weight, picked[matrices:])
    first_new = first_decay * vec_first + (1.0 - first_decay) * grad_share
    second_new = second_decay * vec_second + (1.0 - second_decay) * grad_share * grad_share
    param_new = vec_param - adam_rate * (first_new / first_correct) / (
        jnp.sqrt(second_new / second_correct) + adam_epsilon
    )
    return (
        big_weight_new,
        big_retained[None],
        small_weight_new,
        small_retained[None],
        param_new,
        first_new,
        second_new,
    )


def solution(mesh):
    return jax.shard_map(
        per_device,
        mesh=mesh,
        in_specs=(
            P(None, "shard", "tensor"),
            P(None, "shard", "tensor"),
            P("shard", "tensor", None),
            P(None, "shard", None),
            P(None, "shard", None),
            P("shard", None, None),
            P(),
            P("shard", None),
            P("shard"),
            P("shard"),
            P("shard"),
        ),
        out_specs=(
            P(None, "shard", "tensor"),
            P("shard", "tensor", None),
            P(None, "shard", None),
            P("shard", None, None),
            P("shard"),
            P("shard"),
            P("shard"),
        ),
        check_vma=False,
    )
```

```python
import math

import jax
import jax.numpy as jnp
from jax import lax
from jax.sharding import PartitionSpec as P

D = 1280
ITERS = 2


newton_linear = 3.4445
newton_cubic = -4.775
newton_quintic = 2.0315
momentum_rate = 0.95
muon_rate = 0.05
weight_decay = 0.1
norm_epsilon = 1e-07
adam_rate = 0.004
first_decay = 0.9
second_decay = 0.95
adam_epsilon = 1e-08
first_correct = 0.99997343860111
second_correct = 0.99407947077967


def owner_table(owner_list, count):
    devices = lax.broadcasted_iota(jnp.int32, (count, owner_list.shape[0]), 0)
    return (devices == owner_list[None, :]).astype(jnp.bfloat16)


def route_rows(owner_map, pieces):
    flattened = pieces.reshape(pieces.shape[0], -1)
    routed = jnp.dot(owner_map, flattened, preferred_element_type=jnp.float32)
    return routed.astype(jnp.bfloat16).reshape((owner_map.shape[0],) + pieces.shape[1:])


def collect(owner_map, arrived):
    flattened = arrived.reshape(arrived.shape[0], -1)
    picked = lax.dot_general(
        owner_map, flattened, (((0,), (0,)), ((), ())), preferred_element_type=jnp.float32
    )
    return picked.astype(jnp.bfloat16).reshape((owner_map.shape[1],) + arrived.shape[1:])


def advance(arrived, moment, is_owner):
    gradient = arrived.T.astype(jnp.float32)
    renewed = momentum_rate * moment + gradient
    retained = jnp.where(is_owner, renewed, moment)
    blended = jnp.where(is_owner, gradient + momentum_rate * renewed, 0.0).astype(jnp.bfloat16).T
    return (retained, blended)


def normalized(field):
    values = field.astype(jnp.float32)
    squares = jnp.sum(values * values)
    return (values / (jnp.sqrt(squares) + norm_epsilon)).astype(jnp.bfloat16)


def gram_block(left_part, right_part):
    product = lax.dot_general(
        left_part, right_part, (((0,), (0,)), ((), ())), preferred_element_type=jnp.float32
    )
    return product.astype(jnp.bfloat16)


def poly_block(gram_part, gram_full):
    square = jnp.dot(gram_part, gram_full, preferred_element_type=jnp.float32)
    return (newton_cubic * gram_part.astype(jnp.float32) + newton_quintic * square).astype(
        jnp.bfloat16
    )


def newton_step(column_part, full_iterate, polynomial):
    product = lax.dot_general(
        full_iterate, polynomial, (((1,), (1,)), ((), ())), preferred_element_type=jnp.float32
    )
    return (newton_linear * column_part.astype(jnp.float32) + product).astype(jnp.bfloat16)


def small_newton(field):
    iterate = normalized(field)
    for iteration in range(ITERS):
        gram_full = gram_block(iterate, iterate)
        iterate = newton_step(iterate, iterate, poly_block(gram_full, gram_full))
    return iterate


def apply_update(weight, update):
    scale = 0.2 * math.sqrt(D)
    values = weight.astype(jnp.float32)
    return (
        values - muon_rate * (scale * update.astype(jnp.float32) + weight_decay * values)
    ).astype(jnp.bfloat16)


def gather_columns(column_part):
    count = lax.axis_size("tensor")
    ahead = [(i, (i + 1) % count) for i in range(count)]
    behind = [(i, (i - 1) % count) for i in range(count)]
    from_behind = lax.ppermute(column_part, "tensor", ahead)
    from_ahead = lax.ppermute(column_part, "tensor", behind)
    far = lax.ppermute(from_behind, "tensor", ahead)
    return jnp.concatenate([column_part, from_behind, far, from_ahead], axis=1)


def gather_gram(gram_part):
    return lax.all_gather(gram_part, "tensor", axis=0, tiled=True)


def per_device(
    big_grad,
    big_weight,
    big_moment,
    small_grad,
    small_weight,
    small_moment,
    owners,
    vec_parts,
    vec_param,
    vec_first,
    vec_second,
):
    shards = lax.axis_size("shard")
    shard_place = lax.axis_index("shard")
    column = lax.axis_index("tensor")
    block_width = big_grad.shape[2]
    rows_dev = big_grad.shape[1]
    matrices = big_grad.shape[0]
    joint_map = owner_table(jnp.concatenate([owners[0], owners[1]]), shards)
    joint_pieces = jnp.concatenate([big_grad, small_grad], axis=0)
    routed = route_rows(joint_map, joint_pieces).reshape(shards, -1)
    outgoing = jnp.concatenate(
        [routed, vec_parts[0].astype(jnp.bfloat16).reshape(shards, -1)], axis=1
    )
    incoming = lax.all_to_all(outgoing, "shard", split_axis=0, concat_axis=0, tiled=True)
    arrived = incoming[:, : routed.shape[1]].reshape(shards * rows_dev, block_width)
    grad_share = jnp.sum(incoming[:, routed.shape[1] :].astype(jnp.float32), axis=0)
    big_owner = jnp.any(owners[0] == shard_place)
    small_owner = jnp.any(owners[1] == shard_place)
    big_retained, big_blended = advance(arrived, big_moment[0], big_owner)
    small_retained, small_blended = advance(arrived, small_moment[0], small_owner)
    small_result = small_newton(small_blended)
    full_iterate = normalized(gather_columns(big_blended))
    for iteration in range(ITERS - 1):
        gram_full = gram_block(full_iterate, full_iterate)
        full_iterate = newton_step(full_iterate, full_iterate, poly_block(gram_full, gram_full))
    gram_full = gram_block(full_iterate, full_iterate)
    gram_rows = gram_full[:block_width]
    owned_part = full_iterate[:, :block_width]
    big_result = newton_step(owned_part, full_iterate, poly_block(gram_rows, gram_full))
    own_result = jnp.where(big_owner, big_result, small_result)
    returned = lax.all_to_all(
        own_result.reshape(shards, rows_dev, block_width),
        "shard",
        split_axis=0,
        concat_axis=0,
        tiled=True,
    )
    picked = collect(joint_map, returned)
    big_weight_new = apply_update(big_weight, picked[:matrices])
    small_weight_new = apply_update(small_weight, picked[matrices:])
    first_new = first_decay * vec_first + (1.0 - first_decay) * grad_share
    second_new = second_decay * vec_second + (1.0 - second_decay) * grad_share * grad_share
    param_new = vec_param - adam_rate * (first_new / first_correct) / (
        jnp.sqrt(second_new / second_correct) + adam_epsilon
    )
    return (
        big_weight_new,
        big_retained[None],
        small_weight_new,
        small_retained[None],
        param_new,
        first_new,
        second_new,
    )


def solution(mesh):
    return jax.shard_map(
        per_device,
        mesh=mesh,
        in_specs=(
            P(None, "shard", "tensor"),
            P(None, "shard", "tensor"),
            P("shard", "tensor", None),
            P(None, "shard", None),
            P(None, "shard", None),
            P("shard", None, None),
            P(),
            P("shard", None),
            P("shard"),
            P("shard"),
            P("shard"),
        ),
        out_specs=(
            P(None, "shard", "tensor"),
            P("shard", "tensor", None),
            P(None, "shard", None),
            P("shard", None, None),
            P("shard"),
            P("shard"),
            P("shard"),
        ),
        check_vma=False,
    )
```

```python
import math

import jax
import jax.numpy as jnp
from jax import lax
from jax.sharding import PartitionSpec as P

D = 1280
ITERS = 2


newton_linear = 3.4445
newton_cubic = -4.775
newton_quintic = 2.0315
momentum_rate = 0.95
muon_rate = 0.05
weight_decay = 0.1
norm_epsilon = 1e-07
adam_rate = 0.004
first_decay = 0.9
second_decay = 0.95
adam_epsilon = 1e-08
first_correct = 0.99997343860111
second_correct = 0.99407947077967


def owner_table(owner_list, count):
    devices = lax.broadcasted_iota(jnp.int32, (count, owner_list.shape[0]), 0)
    return (devices == owner_list[None, :]).astype(jnp.bfloat16)


def route_rows(owner_map, pieces):
    flattened = pieces.reshape(pieces.shape[0], -1)
    routed = jnp.dot(owner_map, flattened, preferred_element_type=jnp.float32)
    return routed.astype(jnp.bfloat16).reshape((owner_map.shape[0],) + pieces.shape[1:])


def collect(owner_map, arrived):
    flattened = arrived.reshape(arrived.shape[0], -1)
    picked = lax.dot_general(
        owner_map, flattened, (((0,), (0,)), ((), ())), preferred_element_type=jnp.float32
    )
    return picked.astype(jnp.bfloat16).reshape((owner_map.shape[1],) + arrived.shape[1:])


def advance(arrived, moment, is_owner):
    gradient = arrived.T.astype(jnp.float32)
    renewed = momentum_rate * moment + gradient
    retained = jnp.where(is_owner, renewed, moment)
    blended = jnp.where(is_owner, gradient + momentum_rate * renewed, 0.0).astype(jnp.bfloat16).T
    return (retained, blended)


def normalized(field):
    values = field.astype(jnp.float32)
    squares = jnp.sum(values * values)
    return (values / (jnp.sqrt(squares) + norm_epsilon)).astype(jnp.bfloat16)


def gram_block(left_part, right_part):
    product = lax.dot_general(
        left_part, right_part, (((0,), (0,)), ((), ())), preferred_element_type=jnp.float32
    )
    return product.astype(jnp.bfloat16)


def poly_block(gram_part, gram_full):
    square = jnp.dot(gram_part, gram_full, preferred_element_type=jnp.float32)
    return (newton_cubic * gram_part.astype(jnp.float32) + newton_quintic * square).astype(
        jnp.bfloat16
    )


def newton_step(column_part, full_iterate, polynomial):
    product = lax.dot_general(
        full_iterate, polynomial, (((1,), (1,)), ((), ())), preferred_element_type=jnp.float32
    )
    return (newton_linear * column_part.astype(jnp.float32) + product).astype(jnp.bfloat16)


def small_newton(field):
    iterate = normalized(field)
    for iteration in range(ITERS):
        gram_full = gram_block(iterate, iterate)
        iterate = newton_step(iterate, iterate, poly_block(gram_full, gram_full))
    return iterate


def apply_update(weight, update):
    scale = 0.2 * math.sqrt(D)
    values = weight.astype(jnp.float32)
    return (
        values - muon_rate * (scale * update.astype(jnp.float32) + weight_decay * values)
    ).astype(jnp.bfloat16)


def gather_columns(column_part):
    count = lax.axis_size("tensor")
    ahead = [(i, (i + 1) % count) for i in range(count)]
    behind = [(i, (i - 1) % count) for i in range(count)]
    from_behind = lax.ppermute(column_part, "tensor", ahead)
    from_ahead = lax.ppermute(column_part, "tensor", behind)
    half = column_part.shape[1] // 2
    far_first = lax.ppermute(from_behind[:, :half], "tensor", ahead)
    far_second = lax.ppermute(from_ahead[:, half:], "tensor", behind)
    gathered = jnp.concatenate(
        [column_part, from_behind, far_first, far_second, from_ahead], axis=1
    )
    return gathered


def gather_gram(gram_part):
    return lax.all_gather(gram_part, "tensor", axis=0, tiled=True)


def per_device(
    big_grad,
    big_weight,
    big_moment,
    small_grad,
    small_weight,
    small_moment,
    owners,
    vec_parts,
    vec_param,
    vec_first,
    vec_second,
):
    shards = lax.axis_size("shard")
    shard_place = lax.axis_index("shard")
    column = lax.axis_index("tensor")
    block_width = big_grad.shape[2]
    rows_dev = big_grad.shape[1]
    matrices = big_grad.shape[0]
    joint_map = owner_table(jnp.concatenate([owners[0], owners[1]]), shards)
    joint_pieces = jnp.concatenate([big_grad, small_grad], axis=0)
    routed = route_rows(joint_map, joint_pieces).reshape(shards, -1)
    outgoing = jnp.concatenate(
        [routed, vec_parts[0].astype(jnp.bfloat16).reshape(shards, -1)], axis=1
    )
    incoming = lax.all_to_all(outgoing, "shard", split_axis=0, concat_axis=0, tiled=True)
    arrived = incoming[:, : routed.shape[1]].reshape(shards * rows_dev, block_width)
    grad_share = jnp.sum(incoming[:, routed.shape[1] :].astype(jnp.float32), axis=0)
    big_owner = jnp.any(owners[0] == shard_place)
    small_owner = jnp.any(owners[1] == shard_place)
    big_retained, big_blended = advance(arrived, big_moment[0], big_owner)
    small_retained, small_blended = advance(arrived, small_moment[0], small_owner)
    small_result = small_newton(small_blended)
    full_iterate = normalized(gather_columns(big_blended))
    for iteration in range(ITERS - 1):
        gram_full = gram_block(full_iterate, full_iterate)
        full_iterate = newton_step(full_iterate, full_iterate, poly_block(gram_full, gram_full))
    gram_full = gram_block(full_iterate, full_iterate)
    gram_rows = gram_full[:block_width]
    owned_part = full_iterate[:, :block_width]
    big_result = newton_step(owned_part, full_iterate, poly_block(gram_rows, gram_full))
    own_result = jnp.where(big_owner, big_result, small_result)
    returned = lax.all_to_all(
        own_result.reshape(shards, rows_dev, block_width),
        "shard",
        split_axis=0,
        concat_axis=0,
        tiled=True,
    )
    picked = jnp.take(returned, jnp.concatenate([owners[0], owners[1]]), axis=0)
    big_weight_new = apply_update(big_weight, picked[:matrices])
    small_weight_new = apply_update(small_weight, picked[matrices:])
    first_new = first_decay * vec_first + (1.0 - first_decay) * grad_share
    second_new = second_decay * vec_second + (1.0 - second_decay) * grad_share * grad_share
    param_new = vec_param - adam_rate * (first_new / first_correct) / (
        jnp.sqrt(second_new / second_correct) + adam_epsilon
    )
    return (
        big_weight_new,
        big_retained[None],
        small_weight_new,
        small_retained[None],
        param_new,
        first_new,
        second_new,
    )


def solution(mesh):
    return jax.shard_map(
        per_device,
        mesh=mesh,
        in_specs=(
            P(None, "shard", "tensor"),
            P(None, "shard", "tensor"),
            P("shard", "tensor", None),
            P(None, "shard", None),
            P(None, "shard", None),
            P("shard", None, None),
            P(),
            P("shard", None),
            P("shard"),
            P("shard"),
            P("shard"),
        ),
        out_specs=(
            P(None, "shard", "tensor"),
            P("shard", "tensor", None),
            P(None, "shard", None),
            P("shard", None, None),
            P("shard"),
            P("shard"),
            P("shard"),
        ),
        check_vma=False,
    )
```
